128 devices in a mesh: dp: 16 (over z, x_lo, core), mp: 8 (over y, x_hi).
Axes of the slice: x: 4 (x_hi: 2, x_lo: 2; x = x_hi * 2 + x_lo), y: 4, z: 4, core: 2. Of those that a mesh axis runs over, the one named last changes fastest.
Arguments:
- frozen_input_states: bfloat16 [8192, 8192], P('dp'), may hold values from -6 to 6
- updated_input_states: bfloat16 [8192, 8192], P('dp'), may hold values from -6 to 6
- weight: bfloat16 [8192, 8192], P('dp', 'mp'), may hold values from -0.0625 to 0.0625
- adapter_down_weight: bfloat16 [8192, 64], P('mp'), may hold values from -0.0625 to 0.0625
- adapter_up_weight: bfloat16 [64, 8192], P(None, 'mp'), may hold values from -0.75 to 0.75
- flags: int32 [8192], P('dp'), may hold values from 0 to 1, as said below
- control: float32 [8192], replicated, may hold values from 0.1 to 1
Outputs:
- h_upd: bfloat16 [8192, 8192], P(('dp', 'mp'))
- grad_a: float32 [8192, 64], P('mp')
- grad_b: float32 [64, 8192], P(None, 'mp')
- loss: float32 [1], replicated
The draws below stay inside these ranges and needn't reach their ends.
Inputs may be any that keep to these rules, and one draw needn't show every extreme that they name: `flags`: each data group's share of forget tokens is its own and may lie anywhere between a twentieth and nineteen twentieths.
All inputs are finite; a program needn't handle non-finite values.
Results may differ from the reference program's by a relative error of at most 0.0049.
Values may be sent and summed in bfloat16 or wider, within the bound.
No kernel may reach another device: no remote copies, remote signals or barrier semaphores. Data moves between devices by JAX's collectives and lax.ppermute only.
A program may use at most 128 MiB of HBM per device.

```python
import jax
import jax.numpy as jnp
from jax import lax

MODEL_WIDTH = 8192
ADAPTER_RANK = 64
TOK_G = 512
TOKENS = 8192


def draw_flags(key, part):
    blocks = TOKENS // TOK_G
    side_key = jax.random.fold_in(key, 11)
    size_key = jax.random.fold_in(key, 23)
    score_key = jax.random.fold_in(key, 37)
    side = jax.random.randint(side_key, (blocks,), 0, 2)
    reach = jax.random.randint(size_key, (blocks,), 200, 451)
    rate = 500 + (2 * side - 1) * reach
    place = jnp.arange(TOKENS, dtype=jnp.int32)
    block_of = place // TOK_G
    bar = jnp.take(rate, block_of)
    scores = jax.random.randint(score_key, (TOKENS,), 0, 1000)
    return (scores < bar).astype(jnp.int32)


def shard_levels(rng, extent, split, least, high):
    factor_of, own = 1.0, jax.random.fold_in(rng, 6)
    for dim, parts in split:
        heights = jnp.exp(jax.random.uniform(jax.random.fold_in(own, dim), (parts,), jnp.float32, least / len(split), high / len(split)))
        factor_of = factor_of * jnp.repeat(heights, extent[dim] // parts).reshape([-1 if axis == dim else 1 for axis in range(len(extent))])
    return factor_of


def scatter_about(stream_key, dims, scale, limit, shards=(), held_as=jnp.bfloat16):
    factor_of = shard_levels(stream_key, dims, shards, -0.22, 0.18) if shards else 1.0
    result = jax.random.normal(stream_key, dims, jnp.float32) * scale * factor_of
    return jnp.minimum(jnp.maximum(result, -limit), limit).astype(held_as)


def setup_inputs(seed: int = 0) -> dict:
    key_of = jax.random.split(jax.random.key(seed), 8)
    frozen_input_states = scatter_about(key_of[0], (TOKENS, MODEL_WIDTH), 1.0, 6.0, ((0, 16),))
    updated_input_states = scatter_about(key_of[1], (TOKENS, MODEL_WIDTH), 1.0, 6.0, ((0, 16),))
    weight = scatter_about(key_of[2], (MODEL_WIDTH, MODEL_WIDTH), MODEL_WIDTH ** -0.5, 0.0625, ((0, 16), (1, 8)))
    adapter_down_weight = scatter_about(key_of[3], (MODEL_WIDTH, ADAPTER_RANK), MODEL_WIDTH ** -0.5, 0.0625, ((0, 8),))
    adapter_up_weight = scatter_about(key_of[4], (ADAPTER_RANK, MODEL_WIDTH), ADAPTER_RANK ** -0.5, 0.75, ((1, 8),))
    flags = draw_flags(jax.random.fold_in(key_of[7], 71), 0)
    control = jnp.clip(jax.random.uniform(key_of[6], (MODEL_WIDTH,), jnp.float32, 0.1, 1.0), 0.1, 1.0)
    return dict(frozen_input_states=frozen_input_states, updated_input_states=updated_input_states, weight=weight, adapter_down_weight=adapter_down_weight, adapter_up_weight=adapter_up_weight, flags=flags, control=control)


adapter_gain = 0.5
steer = 90.0
retain_weight = 1.2
loss_multiplier = 65536.0

def reference(frozen_input_states, updated_input_states, weight, adapter_down_weight, adapter_up_weight, flags, control):
    ref_out = jnp.dot(frozen_input_states, weight, preferred_element_type=jnp.float32).astype(jnp.bfloat16)
    frozen_output = jnp.dot(updated_input_states, weight, preferred_element_type=jnp.float32).astype(jnp.bfloat16)
    rank_projection = jnp.dot(updated_input_states, adapter_down_weight, preferred_element_type=jnp.float32).astype(jnp.bfloat16)
    updated_output = frozen_output.astype(jnp.float32) + adapter_gain * jnp.dot(rank_projection, adapter_up_weight, preferred_element_type=jnp.float32)
    unit = control * lax.rsqrt(jnp.sum(control * control) + 1e-06)
    is_forget = flags.astype(jnp.float32)[:, None]
    target = is_forget * steer * unit[None, :] + (1.0 - is_forget) * ref_out.astype(jnp.float32)
    state_difference = updated_output - target
    total_f = jnp.sum(flags).astype(jnp.float32)
    n_forget = jnp.maximum(total_f, 1.0)
    n_retain = jnp.maximum(jnp.asarray(TOKENS, jnp.float32) - total_f, 1.0)
    token_weight = is_forget / n_forget + retain_weight * (1.0 - is_forget) / n_retain
    loss = jnp.sum(token_weight * lax.optimization_barrier(jnp.mean(state_difference * state_difference, axis=1, keepdims=True)))
    output_gradient = (loss_multiplier * 2.0 * adapter_gain / MODEL_WIDTH * token_weight * state_difference).astype(jnp.bfloat16)
    grad_b = jnp.dot(rank_projection.T, output_gradient, preferred_element_type=jnp.float32)
    middle_gradient = jnp.dot(output_gradient, adapter_up_weight.T, preferred_element_type=jnp.float32).astype(jnp.bfloat16)
    grad_a = jnp.dot(updated_input_states.T, middle_gradient, preferred_element_type=jnp.float32)
    return (updated_output.astype(jnp.bfloat16), grad_a, grad_b, loss.reshape(1))
```

```python
import jax
import jax.numpy as jnp
from jax import lax
from jax.sharding import Mesh
from jax.sharding import PartitionSpec as P

adapter_gain = 0.5
steer = 90.0
retain_weight = 1.2
loss_multiplier = 65536.0

DP = ("chip", "core")


def row_adder(source, piece):
    return jnp.dot(source, piece, preferred_element_type=jnp.float32)


def gather_columns(weight):
    cols = weight.shape[1]
    half = cols // 2
    core = lax.axis_index("core")
    pair = lax.all_gather(weight, "core", axis=0, tiled=True)
    mine = lax.dynamic_slice_in_dim(pair, core * half, half, 1)
    rows_half = lax.all_gather(mine, "chip", axis=0, tiled=True)
    both = lax.all_gather(rows_half, "core", axis=0, tiled=False)
    return both


def per_device(
    frozen_input_states,
    updated_input_states,
    weight,
    adapter_down_weight,
    adapter_up_weight,
    flags,
    control,
):
    group = frozen_input_states.shape[0]
    hidden_width = frozen_input_states.shape[1]
    parts = lax.axis_size("mp")
    share = group // parts
    rows_mine = hidden_width // parts
    m = lax.axis_index("mp")

    all_flags = lax.all_gather(flags, DP, axis=0, tiled=True)
    forget_total = jnp.sum(all_flags).astype(jnp.float32)
    all_tokens = jnp.asarray(all_flags.shape[0], jnp.float32)
    n_forget = jnp.maximum(forget_total, 1.0)
    n_retain = jnp.maximum(all_tokens - forget_total, 1.0)

    halves = gather_columns(weight)
    ref_rows = jnp.concatenate(
        [row_adder(frozen_input_states, halves[h]).astype(jnp.bfloat16) for h in range(2)], axis=1
    )
    base_rows = jnp.concatenate(
        [row_adder(updated_input_states, halves[h]).astype(jnp.bfloat16) for h in range(2)], axis=1
    )

    my_rows = lax.dynamic_slice_in_dim(updated_input_states, m * rows_mine, rows_mine, 1)
    low_part = jnp.dot(my_rows, adapter_down_weight, preferred_element_type=jnp.float32)
    rank_projection = lax.psum(low_part, "mp").astype(jnp.bfloat16)

    updated_output = base_rows.astype(jnp.float32) + adapter_gain * jnp.dot(
        rank_projection, adapter_up_weight, preferred_element_type=jnp.float32
    )
    h_upd = lax.all_to_all(
        updated_output.astype(jnp.bfloat16), "mp", split_axis=0, concat_axis=1, tiled=True
    )

    unit = control * lax.rsqrt(jnp.sum(control * control) + 1e-06)
    unit_mine = lax.dynamic_slice_in_dim(unit, m * rows_mine, rows_mine, 0)
    is_forget = flags.astype(jnp.float32)[:, None]
    target = is_forget * steer * unit_mine[None, :] + (1.0 - is_forget) * ref_rows.astype(jnp.float32)
    state_difference = updated_output - target
    token_weight = is_forget / n_forget + retain_weight * (1.0 - is_forget) / n_retain
    local_loss = jnp.sum(
        token_weight * (jnp.sum(state_difference * state_difference, axis=1, keepdims=True) / hidden_width)
    )
    output_gradient = (
        loss_multiplier * 2.0 * adapter_gain / hidden_width * token_weight * state_difference
    ).astype(jnp.bfloat16)
    up_grad = jnp.dot(rank_projection.T, output_gradient, preferred_element_type=jnp.float32)
    middle_part = jnp.dot(output_gradient, adapter_up_weight.T, preferred_element_type=jnp.float32)
    middle_gradient = lax.psum(middle_part, "mp").astype(jnp.bfloat16)
    down_grad = jnp.dot(my_rows.T, middle_gradient, preferred_element_type=jnp.float32)
    down_part, up_part, loss_dp = lax.psum((down_grad, up_grad, local_loss), DP)
    total_loss = lax.psum(loss_dp, "mp")
    return (h_upd, down_part, up_part, total_loss.reshape(1))


def solution(mesh):
    dp_size, mp_size = mesh.devices.shape
    split = Mesh(mesh.devices.reshape(dp_size // 2, 2, mp_size), ("chip", "core", "mp"))
    in_specs = (
        P(DP, None),
        P(DP, None),
        P(DP, "mp"),
        P("mp", None),
        P(None, "mp"),
        P(DP),
        P(),
    )
    out_specs = (P(DP + ("mp",), None), P("mp", None), P(None, "mp"), P())
    return jax.shard_map(
        per_device, mesh=split, in_specs=in_specs, out_specs=out_specs, check_vma=False
    )
```

```python
import jax
import jax.numpy as jnp
from jax import lax
from jax.sharding import PartitionSpec as P

adapter_gain = 0.5
steer = 90.0
retain_weight = 1.2
loss_multiplier = 65536.0

CHUNKS = 2


def row_adder(source, piece):
    return jnp.dot(source, piece, preferred_element_type=jnp.float32)


def per_device(
    frozen_input_states,
    updated_input_states,
    weight,
    adapter_down_weight,
    adapter_up_weight,
    flags,
    control,
):
    group = frozen_input_states.shape[0]
    hidden_width = frozen_input_states.shape[1]
    parts = lax.axis_size("mp")
    rows_mine = hidden_width // parts
    width = rows_mine // CHUNKS
    m = lax.axis_index("mp")

    gathered = [
        lax.all_gather(weight[:, c * width:(c + 1) * width], "dp", axis=0, tiled=True)
        for c in range(CHUNKS)
    ]

    my_rows = lax.dynamic_slice_in_dim(updated_input_states, m * rows_mine, rows_mine, 1)
    low_part = jnp.dot(my_rows, adapter_down_weight, preferred_element_type=jnp.float32)
    rank_projection = lax.psum(low_part, "mp").astype(jnp.bfloat16)

    all_flags = lax.all_gather(flags, "dp", axis=0, tiled=True)
    forget_total = jnp.sum(all_flags).astype(jnp.float32)
    all_tokens = jnp.asarray(all_flags.shape[0], jnp.float32)
    n_forget = jnp.maximum(forget_total, 1.0)
    n_retain = jnp.maximum(all_tokens - forget_total, 1.0)
    is_forget = flags.astype(jnp.float32)[:, None]
    token_weight = is_forget / n_forget + retain_weight * (1.0 - is_forget) / n_retain

    unit = control * lax.rsqrt(jnp.sum(control * control) + 1e-06)
    unit_mine = lax.dynamic_slice_in_dim(unit, m * rows_mine, rows_mine, 0)

    outs, up_grads = [], []
    middle_part = None
    sq_rows = None
    for c in range(CHUNKS):
        cols = slice(c * width, (c + 1) * width)
        up_c = adapter_up_weight[:, cols]
        ref_c = row_adder(frozen_input_states, gathered[c]).astype(jnp.bfloat16)
        base_c = row_adder(updated_input_states, gathered[c]).astype(jnp.bfloat16)
        upd_c = base_c.astype(jnp.float32) + adapter_gain * jnp.dot(
            rank_projection, up_c, preferred_element_type=jnp.float32
        )
        outs.append(upd_c.astype(jnp.bfloat16))
        target = is_forget * steer * unit_mine[None, cols] + (1.0 - is_forget) * ref_c.astype(jnp.float32)
        diff = upd_c - target
        sq = jnp.sum(diff * diff, axis=1, keepdims=True)
        sq_rows = sq if sq_rows is None else sq_rows + sq
        gout = (
            loss_multiplier * 2.0 * adapter_gain / hidden_width * token_weight * diff
        ).astype(jnp.bfloat16)
        up_grads.append(jnp.dot(rank_projection.T, gout, preferred_element_type=jnp.float32))
        mp_c = jnp.dot(gout, up_c.T, preferred_element_type=jnp.float32)
        middle_part = mp_c if middle_part is None else middle_part + mp_c

    h_upd = lax.all_to_all(
        jnp.concatenate(outs, axis=1), "mp", split_axis=0, concat_axis=1, tiled=True
    )
    local_loss = jnp.sum(token_weight * (sq_rows / hidden_width))

    rank = middle_part.shape[1]
    packed = jnp.concatenate(
        [middle_part.reshape(-1), jnp.broadcast_to(local_loss, (128,))]
    )
    packed = lax.psum(packed, "mp")
    middle_gradient = packed[: group * rank].reshape(group, rank).astype(jnp.bfloat16)
    loss_mp = packed[group * rank]

    down_grad = jnp.dot(my_rows.T, middle_gradient, preferred_element_type=jnp.float32)
    up_grad = jnp.concatenate(up_grads, axis=1)
    n_a = down_grad.size
    n_b = up_grad.size
    packed2 = jnp.concatenate(
        [down_grad.reshape(-1), up_grad.reshape(-1), jnp.broadcast_to(loss_mp, (128,))]
    )
    packed2 = lax.psum(packed2, "dp")
    down_part = packed2[:n_a].reshape(down_grad.shape)
    up_part = packed2[n_a:n_a + n_b].reshape(up_grad.shape)
    total_loss = packed2[n_a + n_b]
    return (h_upd, down_part, up_part, total_loss.reshape(1))


def solution(mesh):
    in_specs = (
        P("dp", None),
        P("dp", None),
        P("dp", "mp"),
        P("mp", None),
        P(None, "mp"),
        P("dp"),
        P(),
    )
    out_specs = (P(("dp", "mp"), None), P("mp", None), P(None, "mp"), P())
    return jax.shard_map(
        per_device, mesh=mesh, in_specs=in_specs, out_specs=out_specs, check_vma=False
    )
```

```python
import jax
import jax.numpy as jnp
from jax import lax
from jax.sharding import PartitionSpec as P

adapter_gain = 0.5
steer = 90.0
retain_weight = 1.2
loss_multiplier = 65536.0


def row_adder(source, piece):
    return jnp.dot(source, piece, preferred_element_type=jnp.float32)


def butterfly_sum(x, axis):
    n = lax.axis_size(axis)
    step = 1
    while step < n:
        x = x + lax.ppermute(x, axis, [(i, i ^ step) for i in range(n)])
        step *= 2
    return x


def per_device(
    frozen_input_states,
    updated_input_states,
    weight,
    adapter_down_weight,
    adapter_up_weight,
    flags,
    control,
):
    group = frozen_input_states.shape[0]
    hidden_width = frozen_input_states.shape[1]
    parts = lax.axis_size("mp")
    rows_mine = hidden_width // parts
    m = lax.axis_index("mp")

    gathered = lax.all_gather(weight, "dp", axis=0, tiled=True)

    my_rows = lax.dynamic_slice_in_dim(updated_input_states, m * rows_mine, rows_mine, 1)
    low_part = jnp.dot(my_rows, adapter_down_weight, preferred_element_type=jnp.float32)
    rank_projection = lax.psum(low_part, "mp").astype(jnp.bfloat16)

    all_flags = lax.all_gather(flags, "dp", axis=0, tiled=True)
    forget_total = jnp.sum(all_flags).astype(jnp.float32)
    all_tokens = jnp.asarray(all_flags.shape[0], jnp.float32)
    n_forget = jnp.maximum(forget_total, 1.0)
    n_retain = jnp.maximum(all_tokens - forget_total, 1.0)
    is_forget = flags.astype(jnp.float32)[:, None]
    token_weight = is_forget / n_forget + retain_weight * (1.0 - is_forget) / n_retain

    unit = control * lax.rsqrt(jnp.sum(control * control) + 1e-06)
    unit_mine = lax.dynamic_slice_in_dim(unit, m * rows_mine, rows_mine, 0)

    ref_rows = row_adder(frozen_input_states, gathered).astype(jnp.bfloat16)
    base_rows = row_adder(updated_input_states, gathered).astype(jnp.bfloat16)
    updated_output = base_rows.astype(jnp.float32) + adapter_gain * jnp.dot(
        rank_projection, adapter_up_weight, preferred_element_type=jnp.float32
    )
    h_upd = lax.all_to_all(
        updated_output.astype(jnp.bfloat16), "mp", split_axis=0, concat_axis=1, tiled=True
    )
    target = is_forget * steer * unit_mine[None, :] + (1.0 - is_forget) * ref_rows.astype(jnp.float32)
    state_difference = updated_output - target
    local_loss = jnp.sum(
        token_weight * (jnp.sum(state_difference * state_difference, axis=1, keepdims=True) / hidden_width)
    )
    output_gradient = (
        loss_multiplier * 2.0 * adapter_gain / hidden_width * token_weight * state_difference
    ).astype(jnp.bfloat16)
    up_grad = jnp.dot(rank_projection.T, output_gradient, preferred_element_type=jnp.float32)
    middle_part = jnp.dot(output_gradient, adapter_up_weight.T, preferred_element_type=jnp.float32)

    rank = middle_part.shape[1]
    packed = jnp.concatenate([middle_part, jnp.broadcast_to(local_loss, (8, rank))], axis=0)
    packed = butterfly_sum(packed, "mp")
    middle_gradient = packed[:group].astype(jnp.bfloat16)
    loss_mp = packed[group, 0]

    down_grad = jnp.dot(my_rows.T, middle_gradient, preferred_element_type=jnp.float32)
    n_a = down_grad.size
    n_b = up_grad.size
    packed2 = jnp.concatenate(
        [down_grad.reshape(-1), up_grad.reshape(-1), jnp.broadcast_to(loss_mp, (1024,))]
    )
    packed2 = butterfly_sum(packed2, "dp")
    down_part = packed2[:n_a].reshape(down_grad.shape)
    up_part = packed2[n_a:n_a + n_b].reshape(up_grad.shape)
    total_loss = packed2[n_a + n_b]
    return (h_upd, down_part, up_part, total_loss.reshape(1))


def solution(mesh):
    in_specs = (
        P("dp", None),
        P("dp", None),
        P("dp", "mp"),
        P("mp", None),
        P(None, "mp"),
        P("dp"),
        P(),
    )
    out_specs = (P(("dp", "mp"), None), P("mp", None), P(None, "mp"), P())
    return jax.shard_map(
        per_device, mesh=mesh, in_specs=in_specs, out_specs=out_specs, check_vma=False
    )
```

```python
import jax
import jax.numpy as jnp
from jax import lax
from jax.sharding import PartitionSpec as P

adapter_gain = 0.5
steer = 90.0
retain_weight = 1.2
loss_multiplier = 65536.0


def row_adder(source, piece):
    return jnp.dot(source, piece, preferred_element_type=jnp.float32)


def butterfly_sum(x, axis):
    n = lax.axis_size(axis)
    step = 1
    while step < n:
        x = x + lax.ppermute(x, axis, [(i, i ^ step) for i in range(n)])
        step *= 2
    return x


def send(x, pairs):
    return lax.ppermute(x, "dp", pairs)


def pick(flag, a, b):
    return jnp.where(flag, jnp.concatenate([a, b], axis=0), jnp.concatenate([b, a], axis=0))


def spread_columns(weight):
    n = lax.axis_size("dp")
    rows_blk, cols = weight.shape
    half, quarter = cols // 2, cols // 4
    chip_rows, slab_rows = 2 * rows_blk, 4 * rows_blk
    d = lax.axis_index("dp")
    z, x, c = d // 4, (d // 2) % 2, d % 2
    nz = n // 4
    core_pairs = [(i, i ^ 1) for i in range(n)]
    x_pairs = [(i, i ^ 2) for i in range(n)]
    up_pairs = [(i, ((i // 4 + 1) % nz) * 4 + i % 4) for i in range(n)]
    down_pairs = [(i, ((i // 4 - 1) % nz) * 4 + i % 4) for i in range(n)]

    def chip_at(zz, xx):
        return ((zz % nz) * 2 + xx) * chip_rows

    own = lax.dynamic_slice_in_dim(weight, c * half, half, 1)
    sib = send(lax.dynamic_slice_in_dim(weight, (1 - c) * half, half, 1), core_pairs)
    chip_a = pick(c == 0, own[:, :quarter], sib[:, :quarter])
    chip_b = pick(c == 0, own[:, quarter:], sib[:, quarter:])

    x_a = send(chip_a, x_pairs)
    slab_a = pick(x == 0, chip_a, x_a)
    from_minus = send(slab_a, up_pairs)
    from_plus = send(slab_a, down_pairs)
    far_lo = send(from_minus[:chip_rows], up_pairs)
    far_hi = send(from_plus[chip_rows:], down_pairs)
    pieces_a = [
        (chip_at(z, x), chip_a),
        (chip_at(z, 1 - x), x_a),
        ((z + nz - 1) % nz * slab_rows, from_minus),
        ((z + 1) % nz * slab_rows, from_plus),
        ((z + 2) % nz * slab_rows, far_lo),
        ((z + 2) % nz * slab_rows + chip_rows, far_hi),
    ]

    b_minus = send(chip_b, up_pairs)
    b_plus = send(chip_b, down_pairs)
    b_far_lo = send(b_minus[:rows_blk], up_pairs)
    b_far_hi = send(b_plus[rows_blk:], down_pairs)
    column = jnp.stack([chip_b, b_plus, jnp.concatenate([b_far_lo, b_far_hi], axis=0), b_minus])
    across = send(column, x_pairs)
    pieces_b = [(chip_at(z, x), chip_b), (chip_at(z + 1, x), b_plus),
                (chip_at(z + 2, x), column[2]), (chip_at(z + 3, x), b_minus)]
    pieces_b += [(chip_at(z + r, 1 - x), across[r]) for r in range(4)]

    mine = [(off, blk, 0) for off, blk in pieces_a] + [(off, blk, 1) for off, blk in pieces_b]
    other = [(off, send(blk, core_pairs), q + 2) for off, blk, q in mine]
    return mine + other, c


def project(source, pieces, quarter):
    acc = [None] * 4
    for off, blk, q in pieces:
        part = jnp.dot(
            lax.dynamic_slice_in_dim(source, off, blk.shape[0], 1), blk,
            preferred_element_type=jnp.float32,
        )
        acc[q] = part if acc[q] is None else acc[q] + part
    return acc


def in_order(acc, c):
    mine = jnp.concatenate([acc[0], acc[1]], axis=1)
    other = jnp.concatenate([acc[2], acc[3]], axis=1)
    return jnp.where(c == 0, jnp.concatenate([mine, other], axis=1), jnp.concatenate([other, mine], axis=1))


def per_device(
    frozen_input_states,
    updated_input_states,
    weight,
    adapter_down_weight,
    adapter_up_weight,
    flags,
    control,
):
    group = frozen_input_states.shape[0]
    hidden_width = frozen_input_states.shape[1]
    parts = lax.axis_size("mp")
    rows_mine = hidden_width // parts
    m = lax.axis_index("mp")

    pieces, core = spread_columns(weight)

    my_rows = lax.dynamic_slice_in_dim(updated_input_states, m * rows_mine, rows_mine, 1)
    low_part = jnp.dot(my_rows, adapter_down_weight, preferred_element_type=jnp.float32)
    rank_projection = lax.psum(low_part, "mp").astype(jnp.bfloat16)

    all_flags = lax.all_gather(flags, "dp", axis=0, tiled=True)
    forget_total = jnp.sum(all_flags).astype(jnp.float32)
    all_tokens = jnp.asarray(all_flags.shape[0], jnp.float32)
    n_forget = jnp.maximum(forget_total, 1.0)
    n_retain = jnp.maximum(all_tokens - forget_total, 1.0)
    is_forget = flags.astype(jnp.float32)[:, None]
    token_weight = is_forget / n_forget + retain_weight * (1.0 - is_forget) / n_retain

    unit = control * lax.rsqrt(jnp.sum(control * control) + 1e-06)
    unit_mine = lax.dynamic_slice_in_dim(unit, m * rows_mine, rows_mine, 0)

    ref_rows = in_order(project(frozen_input_states, pieces, 4), core).astype(jnp.bfloat16)
    base_rows = in_order(project(updated_input_states, pieces, 4), core).astype(jnp.bfloat16)
    updated_output = base_rows.astype(jnp.float32) + adapter_gain * jnp.dot(
        rank_projection, adapter_up_weight, preferred_element_type=jnp.float32
    )
    h_upd = lax.all_to_all(
        updated_output.astype(jnp.bfloat16), "mp", split_axis=0, concat_axis=1, tiled=True
    )
    target = is_forget * steer * unit_mine[None, :] + (1.0 - is_forget) * ref_rows.astype(jnp.float32)
    state_difference = updated_output - target
    local_loss = jnp.sum(
        token_weight * (jnp.sum(state_difference * state_difference, axis=1, keepdims=True) / hidden_width)
    )
    output_gradient = (
        loss_multiplier * 2.0 * adapter_gain / hidden_width * token_weight * state_difference
    ).astype(jnp.bfloat16)
    up_grad = jnp.dot(rank_projection.T, output_gradient, preferred_element_type=jnp.float32)
    middle_part = jnp.dot(output_gradient, adapter_up_weight.T, preferred_element_type=jnp.float32)

    rank = middle_part.shape[1]
    packed = jnp.concatenate([middle_part, jnp.broadcast_to(local_loss, (8, rank))], axis=0)
    packed = butterfly_sum(packed, "mp")
    middle_gradient = packed[:group].astype(jnp.bfloat16)
    loss_mp = packed[group, 0]

    down_grad = jnp.dot(my_rows.T, middle_gradient, preferred_element_type=jnp.float32)
    n_a = down_grad.size
    n_b = up_grad.size
    packed2 = jnp.concatenate(
        [down_grad.reshape(-1), up_grad.reshape(-1), jnp.broadcast_to(loss_mp, (1024,))]
    )
    packed2 = butterfly_sum(packed2, "dp")
    down_part = packed2[:n_a].reshape(down_grad.shape)
    up_part = packed2[n_a:n_a + n_b].reshape(up_grad.shape)
    total_loss = packed2[n_a + n_b]
    return (h_upd, down_part, up_part, total_loss.reshape(1))


def solution(mesh):
    in_specs = (
        P("dp", None),
        P("dp", None),
        P("dp", "mp"),
        P("mp", None),
        P(None, "mp"),
        P("dp"),
        P(),
    )
    out_specs = (P(("dp", "mp"), None), P("mp", None), P(None, "mp"), P())
    return jax.shard_map(
        per_device, mesh=mesh, in_specs=in_specs, out_specs=out_specs, check_vma=False
    )
```

```python
import jax
import jax.numpy as jnp
from jax import lax
from jax.sharding import PartitionSpec as P

adapter_gain = 0.5
steer = 90.0
retain_weight = 1.2
loss_multiplier = 65536.0


def row_adder(source, piece):
    return jnp.dot(source, piece, preferred_element_type=jnp.float32)


def butterfly_sum(x, axis):
    n = lax.axis_size(axis)
    step = 1
    while step < n:
        x = x + lax.ppermute(x, axis, [(i, i ^ step) for i in range(n)])
        step *= 2
    return x


def per_device(
    frozen_input_states,
    updated_input_states,
    weight,
    adapter_down_weight,
    adapter_up_weight,
    flags,
    control,
):
    group = frozen_input_states.shape[0]
    hidden_width = frozen_input_states.shape[1]
    parts = lax.axis_size("mp")
    rows_mine = hidden_width // parts
    m = lax.axis_index("mp")

    gathered = lax.all_gather(weight, "dp", axis=0, tiled=True)

    my_rows = lax.dynamic_slice_in_dim(updated_input_states, m * rows_mine, rows_mine, 1)
    low_part = jnp.dot(my_rows, adapter_down_weight, preferred_element_type=jnp.float32)
    rank_projection = lax.psum(low_part, "mp").astype(jnp.bfloat16)

    all_flags = lax.all_gather(flags, "dp", axis=0, tiled=True)
    forget_total = jnp.sum(all_flags).astype(jnp.float32)
    all_tokens = jnp.asarray(all_flags.shape[0], jnp.float32)
    n_forget = jnp.maximum(forget_total, 1.0)
    n_retain = jnp.maximum(all_tokens - forget_total, 1.0)
    is_forget = flags.astype(jnp.float32)[:, None]
    token_weight = is_forget / n_forget + retain_weight * (1.0 - is_forget) / n_retain

    unit = control * lax.rsqrt(jnp.sum(control * control) + 1e-06)
    unit_mine = lax.dynamic_slice_in_dim(unit, m * rows_mine, rows_mine, 0)

    ref_rows = row_adder(frozen_input_states, gathered).astype(jnp.bfloat16)
    base_rows = row_adder(updated_input_states, gathered).astype(jnp.bfloat16)
    updated_output = base_rows.astype(jnp.float32) + adapter_gain * jnp.dot(
        rank_projection, adapter_up_weight, preferred_element_type=jnp.float32
    )
    h_upd = lax.all_to_all(
        updated_output.astype(jnp.bfloat16), "mp", split_axis=0, concat_axis=1, tiled=True
    )
    target = is_forget * steer * unit_mine[None, :] + (1.0 - is_forget) * ref_rows.astype(jnp.float32)
    state_difference = updated_output - target
    local_loss = jnp.sum(
        token_weight * (jnp.sum(state_difference * state_difference, axis=1, keepdims=True) / hidden_width)
    )
    output_gradient = (
        loss_multiplier * 2.0 * adapter_gain / hidden_width * token_weight * state_difference
    ).astype(jnp.bfloat16)
    up_grad = jnp.dot(rank_projection.T, output_gradient, preferred_element_type=jnp.float32)
    middle_part = jnp.dot(output_gradient, adapter_up_weight.T, preferred_element_type=jnp.float32)

    rank = middle_part.shape[1]
    packed = jnp.concatenate([middle_part, jnp.broadcast_to(local_loss, (8, rank))], axis=0)
    packed = butterfly_sum(packed, "mp")
    middle_gradient = packed[:group].astype(jnp.bfloat16)
    loss_mp = packed[group, 0]

    up_part = butterfly_sum(up_grad, "dp")
    down_grad = jnp.dot(my_rows.T, middle_gradient, preferred_element_type=jnp.float32)
    packed2 = jnp.concatenate([down_grad, jnp.broadcast_to(loss_mp, (8, rank))], axis=0)
    packed2 = butterfly_sum(packed2, "dp")
    down_part = packed2[: down_grad.shape[0]]
    total_loss = packed2[down_grad.shape[0], 0]
    return (h_upd, down_part, up_part, total_loss.reshape(1))


def solution(mesh):
    in_specs = (
        P("dp", None),
        P("dp", None),
        P("dp", "mp"),
        P("mp", None),
        P(None, "mp"),
        P("dp"),
        P(),
    )
    out_specs = (P(("dp", "mp"), None), P("mp", None), P(None, "mp"), P())
    return jax.shard_map(
        per_device, mesh=mesh, in_specs=in_specs, out_specs=out_specs, check_vma=False
    )
```

```python
import jax
import jax.numpy as jnp
from jax import lax
from jax.sharding import PartitionSpec as P


adapter_gain = 0.5
steer = 90.0
retain_weight = 1.2
loss_multiplier = 65536.0


def row_adder(source, piece):
    return jnp.dot(source, piece, preferred_element_type=jnp.float32)


def butterfly_sum(x, axis):
    n = lax.axis_size(axis)
    step = 1
    while step < n:
        x = x + lax.ppermute(x, axis, [(i, i ^ step) for i in range(n)])
        step *= 2
    return x


def per_device(
    frozen_input_states,
    updated_input_states,
    weight,
    adapter_down_weight,
    adapter_up_weight,
    flags,
    control,
):
    group = frozen_input_states.shape[0]
    hidden_width = frozen_input_states.shape[1]
    parts = lax.axis_size("mp")
    rows_mine = hidden_width // parts
    m = lax.axis_index("mp")

    cols = weight.shape[1]
    split = cols * 3 // 4
    first = lax.all_gather(weight[:, :split], "dp", axis=0, tiled=True)
    second = lax.all_gather(weight[:, split:], "dp", axis=0, tiled=True)

    my_rows = lax.dynamic_slice_in_dim(updated_input_states, m * rows_mine, rows_mine, 1)
    low_part = jnp.dot(my_rows, adapter_down_weight, preferred_element_type=jnp.float32)
    rank_projection = lax.psum(low_part, "mp").astype(jnp.bfloat16)

    all_flags = lax.all_gather(flags, "dp", axis=0, tiled=True)
    forget_total = jnp.sum(all_flags).astype(jnp.float32)
    all_tokens = jnp.asarray(all_flags.shape[0], jnp.float32)
    n_forget = jnp.maximum(forget_total, 1.0)
    n_retain = jnp.maximum(all_tokens - forget_total, 1.0)
    is_forget = flags.astype(jnp.float32)[:, None]
    token_weight = is_forget / n_forget + retain_weight * (1.0 - is_forget) / n_retain

    unit = control * lax.rsqrt(jnp.sum(control * control) + 1e-06)
    unit_mine = lax.dynamic_slice_in_dim(unit, m * rows_mine, rows_mine, 0)

    ref_rows = jnp.concatenate(
        [row_adder(frozen_input_states, w).astype(jnp.bfloat16) for w in (first, second)], axis=1
    )
    base_rows = jnp.concatenate(
        [row_adder(updated_input_states, w).astype(jnp.bfloat16) for w in (first, second)], axis=1
    )
    updated_output = base_rows.astype(jnp.float32) + adapter_gain * jnp.dot(
        rank_projection, adapter_up_weight, preferred_element_type=jnp.float32
    )
    h_upd = lax.all_to_all(
        updated_output.astype(jnp.bfloat16), "mp", split_axis=0, concat_axis=1, tiled=True
    )
    target = is_forget * steer * unit_mine[None, :] + (1.0 - is_forget) * ref_rows.astype(jnp.float32)
    state_difference = updated_output - target
    local_loss = jnp.sum(
        token_weight * (jnp.sum(state_difference * state_difference, axis=1, keepdims=True) / hidden_width)
    )
    output_gradient = (
        loss_multiplier * 2.0 * adapter_gain / hidden_width * token_weight * state_difference
    ).astype(jnp.bfloat16)
    up_grad = jnp.dot(rank_projection.T, output_gradient, preferred_element_type=jnp.float32)
    middle_part = jnp.dot(output_gradient, adapter_up_weight.T, preferred_element_type=jnp.float32)

    rank = middle_part.shape[1]
    packed = jnp.concatenate([middle_part, jnp.broadcast_to(local_loss, (8, rank))], axis=0)
    packed = butterfly_sum(packed, "mp")
    middle_gradient = packed[:group].astype(jnp.bfloat16)
    loss_mp = packed[group, 0]

    up_part = butterfly_sum(up_grad, "dp")
    down_grad = jnp.dot(my_rows.T, middle_gradient, preferred_element_type=jnp.float32)
    packed2 = jnp.concatenate([down_grad, jnp.broadcast_to(loss_mp, (8, rank))], axis=0)
    packed2 = butterfly_sum(packed2, "dp")
    down_part = packed2[: down_grad.shape[0]]
    total_loss = packed2[down_grad.shape[0], 0]
    return (h_upd, down_part, up_part, total_loss.reshape(1))


def solution(mesh):
    in_specs = (
        P("dp", None),
        P("dp", None),
        P("dp", "mp"),
        P("mp", None),
        P(None, "mp"),
        P("dp"),
        P(),
    )
    out_specs = (P(("dp", "mp"), None), P("mp", None), P(None, "mp"), P())

    return jax.shard_map(per_device, mesh=mesh, in_specs=in_specs, out_specs=out_specs, check_vma=False)
```

```python
import jax
import jax.numpy as jnp
from jax import lax
from jax.sharding import PartitionSpec as P

adapter_gain = 0.5
steer = 90.0
retain_weight = 1.2
loss_multiplier = 65536.0


def row_adder(source, piece):
    return jnp.dot(source, piece, preferred_element_type=jnp.float32)


MASKS = {"dp": (1, 2, 4, 12), "mp": (1, 2, 6)}


def butterfly_sum(x, axis):
    n = lax.axis_size(axis)
    for mask in MASKS[axis]:
        x = x + lax.ppermute(x, axis, [(i, i ^ mask) for i in range(n)])
    return x


def per_device(
    frozen_input_states,
    updated_input_states,
    weight,
    adapter_down_weight,
    adapter_up_weight,
    flags,
    control,
):
    group = frozen_input_states.shape[0]
    hidden_width = frozen_input_states.shape[1]
    parts = lax.axis_size("mp")
    rows_mine = hidden_width // parts
    m = lax.axis_index("mp")

    gathered = lax.all_gather(weight, "dp", axis=0, tiled=True)

    my_rows = lax.dynamic_slice_in_dim(updated_input_states, m * rows_mine, rows_mine, 1)
    low_part = jnp.dot(my_rows, adapter_down_weight, preferred_element_type=jnp.float32)
    rank_projection = lax.psum(low_part, "mp").astype(jnp.bfloat16)

    all_flags = lax.all_gather(flags, "dp", axis=0, tiled=True)
    forget_total = jnp.sum(all_flags).astype(jnp.float32)
    all_tokens = jnp.asarray(all_flags.shape[0], jnp.float32)
    n_forget = jnp.maximum(forget_total, 1.0)
    n_retain = jnp.maximum(all_tokens - forget_total, 1.0)
    is_forget = flags.astype(jnp.float32)[:, None]
    token_weight = is_forget / n_forget + retain_weight * (1.0 - is_forget) / n_retain

    unit = control * lax.rsqrt(jnp.sum(control * control) + 1e-06)
    unit_mine = lax.dynamic_slice_in_dim(unit, m * rows_mine, rows_mine, 0)

    ref_rows = row_adder(frozen_input_states, gathered).astype(jnp.bfloat16)
    base_rows = row_adder(updated_input_states, gathered).astype(jnp.bfloat16)
    updated_output = base_rows.astype(jnp.float32) + adapter_gain * jnp.dot(
        rank_projection, adapter_up_weight, preferred_element_type=jnp.float32
    )
    h_upd = lax.all_to_all(
        updated_output.astype(jnp.bfloat16), "mp", split_axis=0, concat_axis=1, tiled=True
    )
    target = is_forget * steer * unit_mine[None, :] + (1.0 - is_forget) * ref_rows.astype(jnp.float32)
    state_difference = updated_output - target
    local_loss = jnp.sum(
        token_weight * (jnp.sum(state_difference * state_difference, axis=1, keepdims=True) / hidden_width)
    )
    output_gradient = (
        loss_multiplier * 2.0 * adapter_gain / hidden_width * token_weight * state_difference
    ).astype(jnp.bfloat16)
    up_grad = jnp.dot(rank_projection.T, output_gradient, preferred_element_type=jnp.float32)
    middle_part = jnp.dot(output_gradient, adapter_up_weight.T, preferred_element_type=jnp.float32)

    rank = middle_part.shape[1]
    packed = jnp.concatenate([middle_part, jnp.broadcast_to(local_loss, (8, rank))], axis=0)
    packed = butterfly_sum(packed, "mp")
    middle_gradient = packed[:group].astype(jnp.bfloat16)
    loss_mp = packed[group, 0]

    up_part = butterfly_sum(up_grad, "dp")
    down_grad = jnp.dot(my_rows.T, middle_gradient, preferred_element_type=jnp.float32)
    packed2 = jnp.concatenate([down_grad, jnp.broadcast_to(loss_mp, (8, rank))], axis=0)
    packed2 = butterfly_sum(packed2, "dp")
    down_part = packed2[: down_grad.shape[0]]
    total_loss = packed2[down_grad.shape[0], 0]
    return (h_upd, down_part, up_part, total_loss.reshape(1))


def solution(mesh):
    in_specs = (
        P("dp", None),
        P("dp", None),
        P("dp", "mp"),
        P("mp", None),
        P(None, "mp"),
        P("dp"),
        P(),
    )
    out_specs = (P(("dp", "mp"), None), P("mp", None), P(None, "mp"), P())
    return jax.shard_map(
        per_device, mesh=mesh, in_specs=in_specs, out_specs=out_specs, check_vma=False
    )
```

```python
import jax
import jax.numpy as jnp
from jax import lax
from jax.sharding import PartitionSpec as P

adapter_gain = 0.5
steer = 90.0
retain_weight = 1.2
loss_multiplier = 65536.0


def row_adder(source, piece):
    return jnp.dot(source, piece, preferred_element_type=jnp.float32)


MASKS = {"dp": (1, 2, 4, 12), "mp": (1, 2, 6)}


def butterfly_sum(x, axis):
    n = lax.axis_size(axis)
    for mask in MASKS[axis]:
        x = x + lax.ppermute(x, axis, [(i, i ^ mask) for i in range(n)])
    return x


def send(x, pairs):
    return lax.ppermute(x, "dp", pairs)


def pick(flag, a, b):
    return jnp.where(flag, jnp.concatenate([a, b], axis=0), jnp.concatenate([b, a], axis=0))


def spread_columns(weight):
    n = lax.axis_size("dp")
    rows_blk, cols = weight.shape
    half, quarter = cols // 2, cols // 4
    chip_rows, slab_rows = 2 * rows_blk, 4 * rows_blk
    d = lax.axis_index("dp")
    z, x, c = d // 4, (d // 2) % 2, d % 2
    nz = n // 4
    core_pairs = [(i, i ^ 1) for i in range(n)]
    x_pairs = [(i, i ^ 2) for i in range(n)]
    up_pairs = [(i, ((i // 4 + 1) % nz) * 4 + i % 4) for i in range(n)]
    down_pairs = [(i, ((i // 4 - 1) % nz) * 4 + i % 4) for i in range(n)]

    def chip_at(zz, xx):
        return ((zz % nz) * 2 + xx) * chip_rows

    own = lax.dynamic_slice_in_dim(weight, c * half, half, 1)
    sib = send(lax.dynamic_slice_in_dim(weight, (1 - c) * half, half, 1), core_pairs)
    chip_a = pick(c == 0, own[:, :quarter], sib[:, :quarter])
    chip_b = pick(c == 0, own[:, quarter:], sib[:, quarter:])

    x_a = send(chip_a, x_pairs)
    slab_a = pick(x == 0, chip_a, x_a)
    from_minus = send(slab_a, up_pairs)
    from_plus = send(slab_a, down_pairs)
    far_lo = send(from_minus[:chip_rows], up_pairs)
    far_hi = send(from_plus[chip_rows:], down_pairs)
    pieces_a = [
        (chip_at(z, x), chip_a),
        (chip_at(z, 1 - x), x_a),
        ((z + nz - 1) % nz * slab_rows, from_minus),
        ((z + 1) % nz * slab_rows, from_plus),
        ((z + 2) % nz * slab_rows, far_lo),
        ((z + 2) % nz * slab_rows + chip_rows, far_hi),
    ]

    b_minus = send(chip_b, up_pairs)
    b_plus = send(chip_b, down_pairs)
    b_far_lo = send(b_minus[:rows_blk], up_pairs)
    b_far_hi = send(b_plus[rows_blk:], down_pairs)
    column = jnp.stack([chip_b, b_plus, jnp.concatenate([b_far_lo, b_far_hi], axis=0), b_minus])
    across = send(column, x_pairs)
    pieces_b = [(chip_at(z, x), chip_b), (chip_at(z + 1, x), b_plus),
                (chip_at(z + 2, x), column[2]), (chip_at(z + 3, x), b_minus)]
    pieces_b += [(chip_at(z + r, 1 - x), across[r]) for r in range(4)]

    mine = [(off, blk, 0) for off, blk in pieces_a] + [(off, blk, 1) for off, blk in pieces_b]
    other = [(off, send(blk, core_pairs), q + 2) for off, blk, q in mine]
    return mine + other, c


def project(source, pieces, quarter):
    acc = [None] * 4
    for off, blk, q in pieces:
        part = jnp.dot(
            lax.dynamic_slice_in_dim(source, off, blk.shape[0], 1), blk,
            preferred_element_type=jnp.float32,
        )
        acc[q] = part if acc[q] is None else acc[q] + part
    return acc


def in_order(acc, c):
    mine = jnp.concatenate([acc[0], acc[1]], axis=1)
    other = jnp.concatenate([acc[2], acc[3]], axis=1)
    return jnp.where(c == 0, jnp.concatenate([mine, other], axis=1), jnp.concatenate([other, mine], axis=1))


def per_device(
    frozen_input_states,
    updated_input_states,
    weight,
    adapter_down_weight,
    adapter_up_weight,
    flags,
    control,
):
    group = frozen_input_states.shape[0]
    hidden_width = frozen_input_states.shape[1]
    parts = lax.axis_size("mp")
    rows_mine = hidden_width // parts
    m = lax.axis_index("mp")

    pieces, core = spread_columns(weight)

    my_rows = lax.dynamic_slice_in_dim(updated_input_states, m * rows_mine, rows_mine, 1)
    low_part = jnp.dot(my_rows, adapter_down_weight, preferred_element_type=jnp.float32)
    rank_projection = butterfly_sum(low_part, "mp").astype(jnp.bfloat16)

    flag_count = jnp.broadcast_to(jnp.sum(flags), (8, 128))
    forget_total = butterfly_sum(flag_count, "dp")[0, 0].astype(jnp.float32)
    all_tokens = jnp.asarray(flags.shape[0] * lax.axis_size("dp"), jnp.float32)
    n_forget = jnp.maximum(forget_total, 1.0)
    n_retain = jnp.maximum(all_tokens - forget_total, 1.0)
    is_forget = flags.astype(jnp.float32)[:, None]
    token_weight = is_forget / n_forget + retain_weight * (1.0 - is_forget) / n_retain

    unit = control * lax.rsqrt(jnp.sum(control * control) + 1e-06)
    unit_mine = lax.dynamic_slice_in_dim(unit, m * rows_mine, rows_mine, 0)

    ref_rows = in_order(project(frozen_input_states, pieces, 4), core).astype(jnp.bfloat16)
    base_rows = in_order(project(updated_input_states, pieces, 4), core).astype(jnp.bfloat16)
    updated_output = base_rows.astype(jnp.float32) + adapter_gain * jnp.dot(
        rank_projection, adapter_up_weight, preferred_element_type=jnp.float32
    )
    h_upd = lax.all_to_all(
        updated_output.astype(jnp.bfloat16), "mp", split_axis=0, concat_axis=1, tiled=True
    )
    target = is_forget * steer * unit_mine[None, :] + (1.0 - is_forget) * ref_rows.astype(jnp.float32)
    state_difference = updated_output - target
    local_loss = jnp.sum(
        token_weight * (jnp.sum(state_difference * state_difference, axis=1, keepdims=True) / hidden_width)
    )
    output_gradient = (
        loss_multiplier * 2.0 * adapter_gain / hidden_width * token_weight * state_difference
    ).astype(jnp.bfloat16)
    up_grad = jnp.dot(rank_projection.T, output_gradient, preferred_element_type=jnp.float32)
    middle_part = jnp.dot(output_gradient, adapter_up_weight.T, preferred_element_type=jnp.float32)

    rank = middle_part.shape[1]
    packed = jnp.concatenate([middle_part, jnp.broadcast_to(local_loss, (8, rank))], axis=0)
    packed = butterfly_sum(packed, "mp")
    middle_gradient = packed[:group].astype(jnp.bfloat16)
    loss_mp = packed[group, 0]

    up_part = butterfly_sum(up_grad, "dp")
    down_grad = jnp.dot(my_rows.T, middle_gradient, preferred_element_type=jnp.float32)
    packed2 = jnp.concatenate([down_grad, jnp.broadcast_to(loss_mp, (8, rank))], axis=0)
    packed2 = butterfly_sum(packed2, "dp")
    down_part = packed2[: down_grad.shape[0]]
    total_loss = packed2[down_grad.shape[0], 0]
    return (h_upd, down_part, up_part, total_loss.reshape(1))


def solution(mesh):
    in_specs = (
        P("dp", None),
        P("dp", None),
        P("dp", "mp"),
        P("mp", None),
        P(None, "mp"),
        P("dp"),
        P(),
    )
    out_specs = (P(("dp", "mp"), None), P("mp", None), P(None, "mp"), P())
    return jax.shard_map(
        per_device, mesh=mesh, in_specs=in_specs, out_specs=out_specs, check_vma=False
    )
```

```python
import jax
import jax.numpy as jnp
from jax import lax
from jax.sharding import PartitionSpec as P

adapter_gain = 0.5
steer = 90.0
retain_weight = 1.2
loss_multiplier = 65536.0


def row_adder(source, piece):
    return jnp.dot(source, piece, preferred_element_type=jnp.float32)


MASKS = {"dp": (1, 4, 12, 2), "mp": (2, 6, 1)}


def butterfly_sum(x, axis):
    n = lax.axis_size(axis)
    for mask in MASKS[axis]:
        x = x + lax.ppermute(x, axis, [(i, i ^ mask) for i in range(n)])
    return x


def per_device(
    frozen_input_states,
    updated_input_states,
    weight,
    adapter_down_weight,
    adapter_up_weight,
    flags,
    control,
):
    group = frozen_input_states.shape[0]
    hidden_width = frozen_input_states.shape[1]
    parts = lax.axis_size("mp")
    rows_mine = hidden_width // parts
    m = lax.axis_index("mp")

    gathered = lax.all_gather(weight, "dp", axis=0, tiled=True)

    my_rows = lax.dynamic_slice_in_dim(updated_input_states, m * rows_mine, rows_mine, 1)
    low_part = jnp.dot(my_rows, adapter_down_weight, preferred_element_type=jnp.float32)
    rank_projection = lax.psum(low_part, "mp").astype(jnp.bfloat16)

    all_flags = lax.all_gather(flags, "dp", axis=0, tiled=True)
    forget_total = jnp.sum(all_flags).astype(jnp.float32)
    all_tokens = jnp.asarray(all_flags.shape[0], jnp.float32)
    n_forget = jnp.maximum(forget_total, 1.0)
    n_retain = jnp.maximum(all_tokens - forget_total, 1.0)
    is_forget = flags.astype(jnp.float32)[:, None]
    token_weight = is_forget / n_forget + retain_weight * (1.0 - is_forget) / n_retain

    unit = control * lax.rsqrt(jnp.sum(control * control) + 1e-06)
    unit_mine = lax.dynamic_slice_in_dim(unit, m * rows_mine, rows_mine, 0)

    ref_rows = row_adder(frozen_input_states, gathered).astype(jnp.bfloat16)
    base_rows = row_adder(updated_input_states, gathered).astype(jnp.bfloat16)
    updated_output = base_rows.astype(jnp.float32) + adapter_gain * jnp.dot(
        rank_projection, adapter_up_weight, preferred_element_type=jnp.float32
    )
    h_upd = lax.all_to_all(
        updated_output.astype(jnp.bfloat16), "mp", split_axis=0, concat_axis=1, tiled=True
    )
    target = is_forget * steer * unit_mine[None, :] + (1.0 - is_forget) * ref_rows.astype(jnp.float32)
    state_difference = updated_output - target
    local_loss = jnp.sum(
        token_weight * (jnp.sum(state_difference * state_difference, axis=1, keepdims=True) / hidden_width)
    )
    output_gradient = (
        loss_multiplier * 2.0 * adapter_gain / hidden_width * token_weight * state_difference
    ).astype(jnp.bfloat16)
    up_grad = jnp.dot(rank_projection.T, output_gradient, preferred_element_type=jnp.float32)
    middle_part = jnp.dot(output_gradient, adapter_up_weight.T, preferred_element_type=jnp.float32)

    rank = middle_part.shape[1]
    packed = jnp.concatenate([middle_part, jnp.broadcast_to(local_loss, (8, rank))], axis=0)
    packed = butterfly_sum(packed, "mp")
    middle_gradient = packed[:group].astype(jnp.bfloat16)
    loss_mp = packed[group, 0]

    up_part = butterfly_sum(up_grad, "dp")
    down_grad = jnp.dot(my_rows.T, middle_gradient, preferred_element_type=jnp.float32)
    packed2 = jnp.concatenate([down_grad, jnp.broadcast_to(loss_mp, (8, rank))], axis=0)
    packed2 = butterfly_sum(packed2, "dp")
    down_part = packed2[: down_grad.shape[0]]
    total_loss = packed2[down_grad.shape[0], 0]
    return (h_upd, down_part, up_part, total_loss.reshape(1))


def solution(mesh):
    in_specs = (
        P("dp", None),
        P("dp", None),
        P("dp", "mp"),
        P("mp", None),
        P(None, "mp"),
        P("dp"),
        P(),
    )
    out_specs = (P(("dp", "mp"), None), P("mp", None), P(None, "mp"), P())
    return jax.shard_map(
        per_device, mesh=mesh, in_specs=in_specs, out_specs=out_specs, check_vma=False
    )
```

```python
import jax
import jax.numpy as jnp
from jax import lax
from jax.sharding import PartitionSpec as P

adapter_gain = 0.5
steer = 90.0
retain_weight = 1.2
loss_multiplier = 65536.0


def row_adder(source, piece):
    return jnp.dot(source, piece, preferred_element_type=jnp.float32)


MASKS = {"dp": (1, 4, 12, 2), "mp": (2, 6, 1)}


def butterfly_sum(x, axis):
    n = lax.axis_size(axis)
    for mask in MASKS[axis]:
        x = x + lax.ppermute(x, axis, [(i, i ^ mask) for i in range(n)])
    return x


def per_device(
    frozen_input_states,
    updated_input_states,
    weight,
    adapter_down_weight,
    adapter_up_weight,
    flags,
    control,
):
    group = frozen_input_states.shape[0]
    hidden_width = frozen_input_states.shape[1]
    parts = lax.axis_size("mp")
    rows_mine = hidden_width // parts
    m = lax.axis_index("mp")

    gathered = lax.all_gather(weight, "dp", axis=0, tiled=True)

    my_rows = lax.dynamic_slice_in_dim(updated_input_states, m * rows_mine, rows_mine, 1)
    low_part = jnp.dot(my_rows, adapter_down_weight, preferred_element_type=jnp.float32)
    rank_projection = lax.psum(low_part, "mp").astype(jnp.bfloat16)

    all_flags = lax.all_gather(flags, "dp", axis=0, tiled=True)
    forget_total = jnp.sum(all_flags).astype(jnp.float32)
    all_tokens = jnp.asarray(all_flags.shape[0], jnp.float32)
    n_forget = jnp.maximum(forget_total, 1.0)
    n_retain = jnp.maximum(all_tokens - forget_total, 1.0)
    is_forget = flags.astype(jnp.float32)[:, None]
    token_weight = is_forget / n_forget + retain_weight * (1.0 - is_forget) / n_retain

    unit = control * lax.rsqrt(jnp.sum(control * control) + 1e-06)
    unit_mine = lax.dynamic_slice_in_dim(unit, m * rows_mine, rows_mine, 0)

    ref_rows = row_adder(frozen_input_states, gathered).astype(jnp.bfloat16)
    base_rows = row_adder(updated_input_states, gathered).astype(jnp.bfloat16)
    updated_output = base_rows.astype(jnp.float32) + adapter_gain * jnp.dot(
        rank_projection, adapter_up_weight, preferred_element_type=jnp.float32
    )
    h_upd = lax.all_to_all(
        updated_output.astype(jnp.bfloat16), "mp", split_axis=0, concat_axis=1, tiled=True
    )
    target = is_forget * steer * unit_mine[None, :] + (1.0 - is_forget) * ref_rows.astype(jnp.float32)
    state_difference = updated_output - target
    local_loss = jnp.sum(
        token_weight * (jnp.sum(state_difference * state_difference, axis=1, keepdims=True) / hidden_width)
    )
    output_gradient = (
        loss_multiplier * 2.0 * adapter_gain / hidden_width * token_weight * state_difference
    ).astype(jnp.bfloat16)
    up_grad = jnp.dot(rank_projection.T, output_gradient, preferred_element_type=jnp.float32)
    middle_part = jnp.dot(output_gradient, adapter_up_weight.T, preferred_element_type=jnp.float32)

    rank = middle_part.shape[1]
    packed = jnp.concatenate([middle_part, jnp.broadcast_to(local_loss, (8, rank))], axis=0)
    packed = butterfly_sum(packed, "mp")
    middle_gradient = packed[:group].astype(jnp.bfloat16)
    loss_mp = packed[group, 0]

    down_grad = jnp.dot(my_rows.T, middle_gradient, preferred_element_type=jnp.float32)
    rows_a = down_grad.shape[0]
    packed2 = jnp.concatenate(
        [down_grad, up_grad.reshape(-1, rank), jnp.broadcast_to(loss_mp, (8, rank))], axis=0
    )
    packed2 = butterfly_sum(packed2, "dp")
    down_part = packed2[:rows_a]
    up_part = packed2[rows_a:rows_a + up_grad.size // rank].reshape(up_grad.shape)
    total_loss = packed2[rows_a + up_grad.size // rank, 0]
    return (h_upd, down_part, up_part, total_loss.reshape(1))


def solution(mesh):
    in_specs = (
        P("dp", None),
        P("dp", None),
        P("dp", "mp"),
        P("mp", None),
        P(None, "mp"),
        P("dp"),
        P(),
    )
    out_specs = (P(("dp", "mp"), None), P("mp", None), P(None, "mp"), P())
    return jax.shard_map(
        per_device, mesh=mesh, in_specs=in_specs, out_specs=out_specs, check_vma=False
    )
```

```python
import jax
import jax.numpy as jnp
from jax import lax
from jax.sharding import PartitionSpec as P

adapter_gain = 0.5
steer = 90.0
retain_weight = 1.2
loss_multiplier = 65536.0


def row_adder(source, piece):
    return jnp.dot(source, piece, preferred_element_type=jnp.float32)


MASKS = {"dp": (1, 4, 12, 2), "mp": (1, 2, 6)}


def butterfly_sum(x, axis):
    n = lax.axis_size(axis)
    for mask in MASKS[axis]:
        x = x + lax.ppermute(x, axis, [(i, i ^ mask) for i in range(n)])
    return x


def per_device(
    frozen_input_states,
    updated_input_states,
    weight,
    adapter_down_weight,
    adapter_up_weight,
    flags,
    control,
):
    group = frozen_input_states.shape[0]
    hidden_width = frozen_input_states.shape[1]
    parts = lax.axis_size("mp")
    rows_mine = hidden_width // parts
    m = lax.axis_index("mp")

    gathered = lax.all_gather(weight, "dp", axis=0, tiled=True)

    my_rows = lax.dynamic_slice_in_dim(updated_input_states, m * rows_mine, rows_mine, 1)
    low_part = jnp.dot(my_rows, adapter_down_weight, preferred_element_type=jnp.float32)
    rank_projection = lax.psum(low_part, "mp").astype(jnp.bfloat16)

    all_flags = lax.all_gather(flags, "dp", axis=0, tiled=True)
    forget_total = jnp.sum(all_flags).astype(jnp.float32)
    all_tokens = jnp.asarray(all_flags.shape[0], jnp.float32)
    n_forget = jnp.maximum(forget_total, 1.0)
    n_retain = jnp.maximum(all_tokens - forget_total, 1.0)
    is_forget = flags.astype(jnp.float32)[:, None]
    token_weight = is_forget / n_forget + retain_weight * (1.0 - is_forget) / n_retain

    unit = control * lax.rsqrt(jnp.sum(control * control) + 1e-06)
    unit_mine = lax.dynamic_slice_in_dim(unit, m * rows_mine, rows_mine, 0)

    ref_rows = row_adder(frozen_input_states, gathered).astype(jnp.bfloat16)
    base_rows = row_adder(updated_input_states, gathered).astype(jnp.bfloat16)
    updated_output = base_rows.astype(jnp.float32) + adapter_gain * jnp.dot(
        rank_projection, adapter_up_weight, preferred_element_type=jnp.float32
    )
    h_upd = lax.all_to_all(
        updated_output.astype(jnp.bfloat16), "mp", split_axis=0, concat_axis=1, tiled=True
    )
    target = is_forget * steer * unit_mine[None, :] + (1.0 - is_forget) * ref_rows.astype(jnp.float32)
    state_difference = updated_output - target
    local_loss = jnp.sum(
        token_weight * (jnp.sum(state_difference * state_difference, axis=1, keepdims=True) / hidden_width)
    )
    output_gradient = (
        loss_multiplier * 2.0 * adapter_gain / hidden_width * token_weight * state_difference
    ).astype(jnp.bfloat16)
    up_grad = jnp.dot(rank_projection.T, output_gradient, preferred_element_type=jnp.float32)
    middle_part = jnp.dot(output_gradient, adapter_up_weight.T, preferred_element_type=jnp.float32)

    rank = middle_part.shape[1]
    packed = jnp.concatenate([middle_part, jnp.broadcast_to(local_loss, (8, rank))], axis=0)
    packed = butterfly_sum(packed, "mp")
    middle_gradient = packed[:group].astype(jnp.bfloat16)
    loss_mp = packed[group, 0]

    up_part = butterfly_sum(up_grad, "dp")
    down_grad = jnp.dot(my_rows.T, middle_gradient, preferred_element_type=jnp.float32)
    packed2 = jnp.concatenate([down_grad, jnp.broadcast_to(loss_mp, (8, rank))], axis=0)
    packed2 = butterfly_sum(packed2, "dp")
    down_part = packed2[: down_grad.shape[0]]
    total_loss = packed2[down_grad.shape[0], 0]
    return (h_upd, down_part, up_part, total_loss.reshape(1))


def solution(mesh):
    in_specs = (
        P("dp", None),
        P("dp", None),
        P("dp", "mp"),
        P("mp", None),
        P(None, "mp"),
        P("dp"),
        P(),
    )
    out_specs = (P(("dp", "mp"), None), P("mp", None), P(None, "mp"), P())
    return jax.shard_map(
        per_device, mesh=mesh, in_specs=in_specs, out_specs=out_specs, check_vma=False
    )
```

```python
import jax
import jax.numpy as jnp
from jax import lax
from jax.sharding import PartitionSpec as P

adapter_gain = 0.5
steer = 90.0
retain_weight = 1.2
loss_multiplier = 65536.0


def row_adder(source, piece):
    return jnp.dot(source, piece, preferred_element_type=jnp.float32)


MASKS = {"dp": (1, 4, 12, 2), "mp": (2, 6, 1)}


def butterfly_sum(x, axis, masks=None):
    n = lax.axis_size(axis)
    for mask in masks or MASKS[axis]:
        x = x + lax.ppermute(x, axis, [(i, i ^ mask) for i in range(n)])
    return x


def per_device(
    frozen_input_states,
    updated_input_states,
    weight,
    adapter_down_weight,
    adapter_up_weight,
    flags,
    control,
):
    group = frozen_input_states.shape[0]
    hidden_width = frozen_input_states.shape[1]
    parts = lax.axis_size("mp")
    rows_mine = hidden_width // parts
    m = lax.axis_index("mp")

    gathered = lax.all_gather(weight, "dp", axis=0, tiled=True)

    my_rows = lax.dynamic_slice_in_dim(updated_input_states, m * rows_mine, rows_mine, 1)
    low_part = jnp.dot(my_rows, adapter_down_weight, preferred_element_type=jnp.float32)
    rank_projection = lax.psum(low_part, "mp").astype(jnp.bfloat16)

    all_flags = lax.all_gather(flags, "dp", axis=0, tiled=True)
    forget_total = jnp.sum(all_flags).astype(jnp.float32)
    all_tokens = jnp.asarray(all_flags.shape[0], jnp.float32)
    n_forget = jnp.maximum(forget_total, 1.0)
    n_retain = jnp.maximum(all_tokens - forget_total, 1.0)
    is_forget = flags.astype(jnp.float32)[:, None]
    token_weight = is_forget / n_forget + retain_weight * (1.0 - is_forget) / n_retain

    unit = control * lax.rsqrt(jnp.sum(control * control) + 1e-06)
    unit_mine = lax.dynamic_slice_in_dim(unit, m * rows_mine, rows_mine, 0)

    ref_rows = row_adder(frozen_input_states, gathered).astype(jnp.bfloat16)
    base_rows = row_adder(updated_input_states, gathered).astype(jnp.bfloat16)
    updated_output = base_rows.astype(jnp.float32) + adapter_gain * jnp.dot(
        rank_projection, adapter_up_weight, preferred_element_type=jnp.float32
    )
    h_upd = lax.all_to_all(
        updated_output.astype(jnp.bfloat16), "mp", split_axis=0, concat_axis=1, tiled=True
    )
    target = is_forget * steer * unit_mine[None, :] + (1.0 - is_forget) * ref_rows.astype(jnp.float32)
    state_difference = updated_output - target
    local_loss = jnp.sum(
        token_weight * (jnp.sum(state_difference * state_difference, axis=1, keepdims=True) / hidden_width)
    )
    output_gradient = (
        loss_multiplier * 2.0 * adapter_gain / hidden_width * token_weight * state_difference
    ).astype(jnp.bfloat16)
    up_grad = jnp.dot(rank_projection.T, output_gradient, preferred_element_type=jnp.float32)
    middle_part = jnp.dot(output_gradient, adapter_up_weight.T, preferred_element_type=jnp.float32)

    rank = middle_part.shape[1]
    packed = jnp.concatenate([middle_part, jnp.broadcast_to(local_loss, (8, rank))], axis=0)
    packed = butterfly_sum(packed, "mp")
    middle_gradient = packed[:group].astype(jnp.bfloat16)
    loss_mp = packed[group, 0]

    up_part = butterfly_sum(up_grad, "dp", (2, 12, 4, 1))
    down_grad = jnp.dot(my_rows.T, middle_gradient, preferred_element_type=jnp.float32)
    packed2 = jnp.concatenate([down_grad, jnp.broadcast_to(loss_mp, (8, rank))], axis=0)
    packed2 = butterfly_sum(packed2, "dp")
    down_part = packed2[: down_grad.shape[0]]
    total_loss = packed2[down_grad.shape[0], 0]
    return (h_upd, down_part, up_part, total_loss.reshape(1))


def solution(mesh):
    in_specs = (
        P("dp", None),
        P("dp", None),
        P("dp", "mp"),
        P("mp", None),
        P(None, "mp"),
        P("dp"),
        P(),
    )
    out_specs = (P(("dp", "mp"), None), P("mp", None), P(None, "mp"), P())
    return jax.shard_map(
        per_device, mesh=mesh, in_specs=in_specs, out_specs=out_specs, check_vma=False
    )
```

```python
import jax
import jax.numpy as jnp
from jax import lax
from jax.sharding import PartitionSpec as P

adapter_gain = 0.5
steer = 90.0
retain_weight = 1.2
loss_multiplier = 65536.0


def row_adder(source, piece):
    return jnp.dot(source, piece, preferred_element_type=jnp.float32)


MASKS = {"dp": (1, 4, 12, 2), "mp": (2, 6, 1)}


def butterfly_sum(x, axis, masks=None):
    n = lax.axis_size(axis)
    for mask in masks or MASKS[axis]:
        x = x + lax.ppermute(x, axis, [(i, i ^ mask) for i in range(n)])
    return x


def per_device(
    frozen_input_states,
    updated_input_states,
    weight,
    adapter_down_weight,
    adapter_up_weight,
    flags,
    control,
):
    group = frozen_input_states.shape[0]
    hidden_width = frozen_input_states.shape[1]
    parts = lax.axis_size("mp")
    rows_mine = hidden_width // parts
    m = lax.axis_index("mp")

    gathered = lax.all_gather(weight, "dp", axis=0, tiled=True)

    my_rows = lax.dynamic_slice_in_dim(updated_input_states, m * rows_mine, rows_mine, 1)
    low_part = jnp.dot(my_rows, adapter_down_weight, preferred_element_type=jnp.float32)
    rank_projection = lax.psum(low_part, "mp").astype(jnp.bfloat16)

    all_flags = lax.all_gather(flags, "dp", axis=0, tiled=True)
    forget_total = jnp.sum(all_flags).astype(jnp.float32)
    all_tokens = jnp.asarray(all_flags.shape[0], jnp.float32)
    n_forget = jnp.maximum(forget_total, 1.0)
    n_retain = jnp.maximum(all_tokens - forget_total, 1.0)
    is_forget = flags.astype(jnp.float32)[:, None]
    token_weight = is_forget / n_forget + retain_weight * (1.0 - is_forget) / n_retain

    unit = control * lax.rsqrt(jnp.sum(control * control) + 1e-06)
    unit_mine = lax.dynamic_slice_in_dim(unit, m * rows_mine, rows_mine, 0)

    ref_rows = row_adder(frozen_input_states, gathered).astype(jnp.bfloat16)
    base_rows = row_adder(updated_input_states, gathered).astype(jnp.bfloat16)
    updated_output = base_rows.astype(jnp.float32) + adapter_gain * jnp.dot(
        rank_projection, adapter_up_weight, preferred_element_type=jnp.float32
    )
    h_upd = lax.all_to_all(
        updated_output.astype(jnp.bfloat16), "mp", split_axis=0, concat_axis=1, tiled=True
    )
    target = is_forget * steer * unit_mine[None, :] + (1.0 - is_forget) * ref_rows.astype(jnp.float32)
    state_difference = updated_output - target
    local_loss = jnp.sum(
        token_weight * (jnp.sum(state_difference * state_difference, axis=1, keepdims=True) / hidden_width)
    )
    output_gradient = (
        loss_multiplier * 2.0 * adapter_gain / hidden_width * token_weight * state_difference
    ).astype(jnp.bfloat16)
    up_grad = jnp.dot(rank_projection.T, output_gradient, preferred_element_type=jnp.float32)
    middle_part = jnp.dot(output_gradient, adapter_up_weight.T, preferred_element_type=jnp.float32)

    rank = middle_part.shape[1]
    packed = jnp.concatenate([middle_part, jnp.broadcast_to(local_loss, (8, rank))], axis=0)
    packed = butterfly_sum(packed, "mp")
    middle_gradient = packed[:group].astype(jnp.bfloat16)
    loss_mp = packed[group, 0]

    up_part = butterfly_sum(up_grad, "dp", (4, 12, 2, 1))
    down_grad = jnp.dot(my_rows.T, middle_gradient, preferred_element_type=jnp.float32)
    packed2 = jnp.concatenate([down_grad, jnp.broadcast_to(loss_mp, (8, rank))], axis=0)
    packed2 = butterfly_sum(packed2, "dp")
    down_part = packed2[: down_grad.shape[0]]
    total_loss = packed2[down_grad.shape[0], 0]
    return (h_upd, down_part, up_part, total_loss.reshape(1))


def solution(mesh):
    in_specs = (
        P("dp", None),
        P("dp", None),
        P("dp", "mp"),
        P("mp", None),
        P(None, "mp"),
        P("dp"),
        P(),
    )
    out_specs = (P(("dp", "mp"), None), P("mp", None), P(None, "mp"), P())
    return jax.shard_map(
        per_device, mesh=mesh, in_specs=in_specs, out_specs=out_specs, check_vma=False
    )
```
